128 devices in a mesh: dp: 32 (over y, x, core), proto: 4 (over z).
Axes of the slice: x: 4, y: 4, z: 4, core: 2. Of those that a mesh axis runs over, the one named last changes fastest.
Arguments:
- features: bfloat16 [16384, 2048], P('dp', 'proto'), may hold values from -8 to 8
- head_weight: bfloat16 [2048, 256], P('proto'), may hold values from -1 to 1
- prototypes: bfloat16 [256, 32768], P(None, 'proto'), may hold values from -1 to 1
Outputs:
- codes: bfloat16 [16384, 32768], P('dp', 'proto')
- proto_grad: float32 [256, 32768], P('dp', 'proto')
- head_grad: float32 [256, 2048], P('dp', 'proto')
The draws below stay inside these ranges and needn't reach their ends.
All inputs are finite; a program needn't handle non-finite values.
Results may differ from the reference program's by a relative error of at most 0.009.
Values may be sent and summed in bfloat16 or wider, within the bound.
No kernel may reach another device: no remote copies, remote signals or barrier semaphores. Data moves between devices by JAX's collectives and lax.ppermute only.
A program may use at most 128 MiB of HBM per device.

```python
import jax
import jax.numpy as jnp
from jax import lax

IN = 2048
EMB = 256
PROTOS = 32768
ITERS = 3
TOKENS = 16384


def common_dirs(key):
    key_in = jax.random.fold_in(key, 21)
    key_emb = jax.random.fold_in(key, 22)
    dirs_in = jnp.where(jax.random.bernoulli(key_in, 0.5, (4, IN)), 1.0, -1.0).astype(jnp.float32)
    signs = jnp.where(jax.random.bernoulli(key_emb, 0.5, (EMB,)), 1.0, -1.0).astype(jnp.float32)
    coord = jnp.arange(EMB) // (EMB // 4)
    member = (coord[None, :] == jnp.arange(4)[:, None]).astype(jnp.float32)
    dirs_emb = member * signs[None, :] / jnp.sqrt(jnp.float32(EMB // 4))
    return (dirs_in, dirs_emb)


def draw_features(key, part):
    key_mean = jax.random.fold_in(key, 11)
    key_noise = jax.random.fold_in(key, 12)
    key_group = jax.random.fold_in(key, 14)
    dirs_in, dirs_emb = common_dirs(key)
    group = jax.random.randint(key_group, (TOKENS,), 0, 4)
    shared = 0.5 * jax.random.normal(key_mean, (IN,), jnp.float32)
    values = jax.random.normal(key_noise, (TOKENS, IN), jnp.float32) + 0.8 * dirs_in[group] + shared[None, :]
    return jnp.clip(values, -8.0, 8.0).astype(jnp.bfloat16)


def draw_head_weight(key, part):
    key_noise = jax.random.fold_in(key, 31)
    dirs_in, dirs_emb = common_dirs(key)
    noise = jax.random.normal(key_noise, (IN, EMB), jnp.float32) / jnp.sqrt(jnp.float32(IN))
    coupling = jnp.sqrt(jnp.float32(EMB)) / (0.8 * IN)
    signal = jnp.sum(dirs_in[:, :, None] * dirs_emb[:, None, :], axis=0)
    return jnp.clip(noise + coupling * signal, -1.0, 1.0).astype(jnp.bfloat16)


def draw_prototypes(key, part):
    key_noise = jax.random.fold_in(key, 41)
    dirs_in, dirs_emb = common_dirs(key)
    noise = jax.random.normal(key_noise, (EMB, PROTOS), jnp.float32) / jnp.sqrt(jnp.float32(EMB))
    block = jnp.arange(PROTOS) * 4 // PROTOS
    strength = 0.15 * (block.astype(jnp.float32) + 1.0)
    values = noise + strength[None, :] * dirs_emb[block].T
    return jnp.clip(values, -1.0, 1.0).astype(jnp.bfloat16)


def setup_inputs(seed: int = 0) -> dict:
    key_of = jax.random.split(jax.random.key(seed), 4)
    features = draw_features(jax.random.fold_in(key_of[3], 71), 0)
    head_weight = draw_head_weight(jax.random.fold_in(key_of[3], 71), 0)
    prototypes = draw_prototypes(jax.random.fold_in(key_of[3], 71), 0)
    return dict(features=features, head_weight=head_weight, prototypes=prototypes)


sink_eps = 0.05
soft_temp = 0.1

def reference(features, head_weight, prototypes):
    projected = jnp.dot(features, head_weight, preferred_element_type=jnp.float32)
    length = jnp.sqrt(lax.optimization_barrier(jnp.sum(projected * projected, axis=1, keepdims=True)) + 1e-06)
    unit = projected / length
    unit_b = unit.astype(jnp.bfloat16)
    proto_f = prototypes.astype(jnp.float32)
    normed = (proto_f / jnp.sqrt(lax.optimization_barrier(jnp.sum(proto_f * proto_f, axis=0, keepdims=True)) + 1e-06)).astype(jnp.bfloat16)
    scores = jnp.dot(unit_b, normed, preferred_element_type=jnp.float32)
    col_scale = jnp.ones((PROTOS,), jnp.float32)
    row_scale = jnp.ones((TOKENS,), jnp.float32)
    for step in range(ITERS):
        col_sum = lax.optimization_barrier(jnp.sum(jnp.exp(scores / sink_eps) * col_scale[None, :] * row_scale[:, None], axis=0))
        col_scale = col_scale / col_sum
        row_sum = lax.optimization_barrier(jnp.sum(jnp.exp(scores / sink_eps) * col_scale[None, :] * row_scale[:, None], axis=1))
        row_scale = row_scale / row_sum
    plan = jnp.exp(scores / sink_eps) * col_scale[None, :] * row_scale[:, None]
    soft = jnp.exp(scores / soft_temp)
    probs = soft / lax.optimization_barrier(jnp.sum(soft, axis=1, keepdims=True))
    codes = (PROTOS * plan).astype(jnp.bfloat16)
    factor = PROTOS / (soft_temp * jnp.sqrt(jnp.float32(TOKENS)))
    dscore = ((probs - plan) * factor).astype(jnp.bfloat16)
    proto_grad = lax.dot_general(unit_b, dscore, (((0,), (0,)), ((), ())), preferred_element_type=jnp.float32)
    dunit = lax.dot_general(dscore, normed, (((1,), (1,)), ((), ())), preferred_element_type=jnp.float32)
    dproj = ((dunit - unit * lax.optimization_barrier(jnp.sum(unit * dunit, axis=1, keepdims=True))) / length).astype(jnp.bfloat16)
    head_grad = lax.dot_general(dproj, features, (((0,), (0,)), ((), ())), preferred_element_type=jnp.float32)
    return (codes, proto_grad, head_grad)
```

```python
import math

import jax
import jax.numpy as jnp
from jax import lax
from jax.sharding import Mesh
from jax.sharding import PartitionSpec as P

PROTOS = 32768
ITERS = 3


sink_eps = 0.05
soft_temp = 0.1

DP = ("y", "x", "core")
SIZES = {"y": 4, "x": 4, "core": 2, "z": 4}
F32 = jnp.float32
BF16 = jnp.bfloat16


def _shift(v, ax, k):
    n = SIZES[ax]
    return lax.ppermute(v, ax, [(i, (i + k) % n) for i in range(n)])


def _allsum(v, ax, dt=None):
    sent = v if dt is None else v.astype(dt)
    acc = v
    for k in range(1, SIZES[ax]):
        acc = acc + _shift(sent, ax, k).astype(v.dtype)
    return acc


def _allsum_dp(v):
    for ax in ("core", "x", "y"):
        v = _allsum(v, ax)
    return v


def _rs(a, ax, axis, dt=None):
    n = SIZES[ax]
    i = lax.axis_index(ax)
    acc = lax.dynamic_index_in_dim(a, i, axis, keepdims=False)
    for k in range(1, n):
        blk = lax.dynamic_index_in_dim(a, (i + k) % n, axis, keepdims=False)
        if dt is not None:
            blk = blk.astype(dt)
        acc = acc + _shift(blk, ax, k).astype(a.dtype)
    return acc


def _ag(v, ax):
    n = SIZES[ax]
    i = lax.axis_index(ax)
    parts = [v] + [_shift(v, ax, k) for k in range(1, n)]
    rel = jnp.stack(parts)
    idx = (i - jnp.arange(n)) % n
    return rel[idx]


def _rs_dp(part, dt):
    R, N = part.shape
    a = part.reshape(SIZES["y"], SIZES["x"], SIZES["core"], R // 32, N)
    a = _rs(a, "core", 2, dt)
    a = _rs(a, "x", 1, dt)
    a = _rs(a, "y", 0, dt)
    return a


def on_device(features, head_weight, prototypes):
    partial_proj = jnp.dot(features, head_weight, preferred_element_type=F32)
    T, E = partial_proj.shape
    nz = SIZES["z"]
    proj_blk = _rs(partial_proj.reshape(nz, T // nz, E), "z", 0)
    projected = _ag(proj_blk, "z").reshape(T, E)
    length = jnp.sqrt(jnp.sum(projected * projected, axis=1, keepdims=True) + 1e-06)
    unit = projected / length
    unit_b = unit.astype(BF16)
    proto_f = prototypes.astype(F32)
    normed = (proto_f / jnp.sqrt(jnp.sum(proto_f * proto_f, axis=0, keepdims=True) + 1e-06)).astype(BF16)
    scores = jnp.dot(unit_b, normed, preferred_element_type=F32)
    kern = jnp.exp(scores / sink_eps)
    soft = jnp.exp(scores / soft_temp)
    soft_local = jnp.sum(soft, axis=1)
    r = None
    soft_total = None
    for step in range(ITERS):
        colpart = jnp.sum(kern if r is None else kern * r[:, None], axis=0)
        c = 1.0 / _allsum_dp(colpart)
        rowpart = jnp.sum(kern * c[None, :], axis=1)
        if step == 0:
            both = _allsum(jnp.stack([rowpart, soft_local]), "z")
            row, soft_total = both[0], both[1]
        else:
            row = _allsum(rowpart, "z")
        r = 1.0 / row
    plan = kern * c[None, :] * r[:, None]
    probs = soft / soft_total[:, None]
    codes = (PROTOS * plan).astype(BF16)
    tokens_all = 32 * T
    factor = PROTOS / (soft_temp * math.sqrt(tokens_all))
    dscore = ((probs - plan) * factor).astype(BF16)
    pg_part = lax.dot_general(unit_b, dscore, (((0,), (0,)), ((), ())), preferred_element_type=F32)
    proto_grad = _rs_dp(pg_part, BF16)
    dunit_part = lax.dot_general(dscore, normed, (((1,), (1,)), ((), ())), preferred_element_type=F32)
    dunit = _allsum(dunit_part, "z", BF16)
    dproj = ((dunit - unit * jnp.sum(unit * dunit, axis=1, keepdims=True)) / length).astype(BF16)
    head_part = lax.dot_general(dproj, features, (((0,), (0,)), ((), ())), preferred_element_type=F32)
    head_grad = _rs_dp(head_part, BF16)
    return (codes, proto_grad, head_grad)


def solution(mesh):
    devs = mesh.devices.reshape(SIZES["y"], SIZES["x"], SIZES["core"], SIZES["z"])
    m4 = Mesh(devs, ("y", "x", "core", "z"))
    in_specs = (P(DP, "z"), P("z", None), P(None, "z"))
    out_specs = (P(DP, "z"), P(DP, "z"), P(DP, "z"))
    return jax.shard_map(on_device, mesh=m4, in_specs=in_specs, out_specs=out_specs, check_vma=False)
```

```python
import math

import jax
import jax.numpy as jnp
from jax import lax
from jax.sharding import Mesh
from jax.sharding import PartitionSpec as P

PROTOS = 32768
ITERS = 3


sink_eps = 0.05
soft_temp = 0.1

DP = ("y", "x", "core")
SIZES = {"y": 4, "x": 4, "core": 2, "z": 4}
F32 = jnp.float32
BF16 = jnp.bfloat16


def _shift(v, ax, k):
    n = SIZES[ax]
    return lax.ppermute(v, ax, [(i, (i + k) % n) for i in range(n)])


def _allsum(v, ax, dt=None):
    sent = v if dt is None else v.astype(dt)
    acc = v
    for k in range(1, SIZES[ax]):
        acc = acc + _shift(sent, ax, k).astype(v.dtype)
    return acc


def _allsum_dp(v):
    for ax in ("core", "x", "y"):
        v = _allsum(v, ax)
    return v


def _rs(a, ax, axis, dt=None):
    n = SIZES[ax]
    i = lax.axis_index(ax)
    acc = lax.dynamic_index_in_dim(a, i, axis, keepdims=False)
    for k in range(1, n):
        blk = lax.dynamic_index_in_dim(a, (i + k) % n, axis, keepdims=False)
        if dt is not None:
            blk = blk.astype(dt)
        acc = acc + _shift(blk, ax, k).astype(a.dtype)
    return acc


def _ag(v, ax):
    n = SIZES[ax]
    i = lax.axis_index(ax)
    parts = [v] + [_shift(v, ax, k) for k in range(1, n)]
    rel = jnp.stack(parts)
    idx = (i - jnp.arange(n)) % n
    return rel[idx]


def _rs_dp(part, dt):
    R, N = part.shape
    a = part.reshape(SIZES["y"], SIZES["x"], SIZES["core"], R // 32, N)
    a = _rs(a, "core", 2, dt)
    a = _rs(a, "x", 1, dt)
    a = _rs(a, "y", 0, dt)
    return a


def on_device(features, head_weight, prototypes):
    partial_proj = jnp.dot(features, head_weight, preferred_element_type=F32)
    T, E = partial_proj.shape
    nz = SIZES["z"]
    proj_blk = _rs(partial_proj.reshape(nz, T // nz, E), "z", 0)
    projected = _ag(proj_blk, "z").reshape(T, E)
    length = jnp.sqrt(jnp.sum(projected * projected, axis=1, keepdims=True) + 1e-06)
    unit = projected / length
    unit_b = unit.astype(BF16)
    proto_f = prototypes.astype(F32)
    normed = (proto_f / jnp.sqrt(jnp.sum(proto_f * proto_f, axis=0, keepdims=True) + 1e-06)).astype(BF16)
    scores = jnp.dot(unit_b, normed, preferred_element_type=F32)
    soft = lax.optimization_barrier(jnp.exp(scores / soft_temp))
    kern = soft * soft
    soft_local = jnp.sum(soft, axis=1)
    r = None
    soft_total = None
    for step in range(ITERS):
        colpart = jnp.sum(kern if r is None else kern * r[:, None], axis=0)
        c = 1.0 / _allsum_dp(colpart)
        rowpart = jnp.sum(kern * c[None, :], axis=1)
        if step == 0:
            both = _allsum(jnp.stack([rowpart, soft_local]), "z")
            row, soft_total = both[0], both[1]
        else:
            row = _allsum(rowpart, "z")
        r = 1.0 / row
    plan = kern * c[None, :] * r[:, None]
    probs = soft / soft_total[:, None]
    codes = (PROTOS * plan).astype(BF16)
    tokens_all = 32 * T
    factor = PROTOS / (soft_temp * math.sqrt(tokens_all))
    dscore = ((probs - plan) * factor).astype(BF16)
    half = dscore.shape[1] // 2
    pg = []
    for h in range(2):
        pg_part = lax.dot_general(
            unit_b, dscore[:, h * half:(h + 1) * half], (((0,), (0,)), ((), ())), preferred_element_type=F32
        )
        pg.append(_rs_dp(pg_part, BF16))
    proto_grad = jnp.concatenate(pg, axis=1)
    dunit_part = lax.dot_general(dscore, normed, (((1,), (1,)), ((), ())), preferred_element_type=F32)
    dunit = _allsum(dunit_part, "z", BF16)
    dproj = ((dunit - unit * jnp.sum(unit * dunit, axis=1, keepdims=True)) / length).astype(BF16)
    head_part = lax.dot_general(dproj, features, (((0,), (0,)), ((), ())), preferred_element_type=F32)
    head_grad = _rs_dp(head_part, BF16)
    return (codes, proto_grad, head_grad)


def solution(mesh):
    devs = mesh.devices.reshape(SIZES["y"], SIZES["x"], SIZES["core"], SIZES["z"])
    m4 = Mesh(devs, ("y", "x", "core", "z"))
    in_specs = (P(DP, "z"), P("z", None), P(None, "z"))
    out_specs = (P(DP, "z"), P(DP, "z"), P(DP, "z"))
    return jax.shard_map(on_device, mesh=m4, in_specs=in_specs, out_specs=out_specs, check_vma=False)
```

```python
import math

import jax
import jax.numpy as jnp
from jax import lax
from jax.experimental import pallas as pl
from jax.sharding import Mesh
from jax.sharding import PartitionSpec as P

PROTOS = 32768
ITERS = 3


sink_eps = 0.05
soft_temp = 0.1

DP = ("y", "x", "core")
SIZES = {"y": 4, "x": 4, "core": 2, "z": 4}
F32 = jnp.float32
BF16 = jnp.bfloat16


def _shift(v, ax, k):
    n = SIZES[ax]
    return lax.ppermute(v, ax, [(i, (i + k) % n) for i in range(n)])


def _allsum(v, ax, dt=None):
    sent = v if dt is None else v.astype(dt)
    acc = v
    for k in range(1, SIZES[ax]):
        acc = acc + _shift(sent, ax, k).astype(v.dtype)
    return acc


def _allsum_dp(v):
    for ax in ("core", "x", "y"):
        v = _allsum(v, ax)
    return v


def _rs(a, ax, axis, dt=None):
    n = SIZES[ax]
    i = lax.axis_index(ax)
    acc = lax.dynamic_index_in_dim(a, i, axis, keepdims=False)
    for k in range(1, n):
        blk = lax.dynamic_index_in_dim(a, (i + k) % n, axis, keepdims=False)
        if dt is not None:
            blk = blk.astype(dt)
        acc = acc + _shift(blk, ax, k).astype(a.dtype)
    return acc


def _ag(v, ax):
    n = SIZES[ax]
    i = lax.axis_index(ax)
    parts = [v] + [_shift(v, ax, k) for k in range(1, n)]
    rel = jnp.stack(parts)
    idx = (i - jnp.arange(n)) % n
    return rel[idx]


def _rs_dp(part, dt):
    R, N = part.shape
    a = part.reshape(SIZES["y"], SIZES["x"], SIZES["core"], R // 32, N)
    a = _rs(a, "core", 2, dt)
    a = _rs(a, "x", 1, dt)
    a = _rs(a, "y", 0, dt)
    return a


def _score_kernel(u_ref, n_ref, s_ref, col_ref, rs_ref):
    j = pl.program_id(0)
    sc = jnp.dot(u_ref[...], n_ref[...], preferred_element_type=F32)
    s = jnp.exp(sc * (1.0 / soft_temp))
    s_ref[...] = s
    col_ref[...] = jnp.sum(s * s, axis=0, keepdims=True)

    @pl.when(j == 0)
    def _():
        rs_ref[...] = jnp.zeros_like(rs_ref)

    rs_ref[...] += jnp.sum(s, axis=1, keepdims=True)


def _scores(unit_b, normed, bp=1024):
    T, E = unit_b.shape
    Pn = normed.shape[1]
    soft, col, rs = pl.pallas_call(
        _score_kernel,
        grid=(Pn // bp,),
        in_specs=[pl.BlockSpec((T, E), lambda j: (0, 0)), pl.BlockSpec((E, bp), lambda j: (0, j))],
        out_specs=[
            pl.BlockSpec((T, bp), lambda j: (0, j)),
            pl.BlockSpec((1, bp), lambda j: (0, j)),
            pl.BlockSpec((T, 1), lambda j: (0, 0)),
        ],
        out_shape=[
            jax.ShapeDtypeStruct((T, Pn), F32),
            jax.ShapeDtypeStruct((1, Pn), F32),
            jax.ShapeDtypeStruct((T, 1), F32),
        ],
    )(unit_b, normed)
    return soft, col[0], rs[:, 0]


def _col_kernel(s_ref, r_ref, o_ref):
    s = s_ref[...]
    o_ref[...] = jnp.sum(s * s * r_ref[...], axis=0, keepdims=True)


def _colpass(soft, r, bp=1024):
    T, Pn = soft.shape
    return pl.pallas_call(
        _col_kernel,
        grid=(Pn // bp,),
        in_specs=[pl.BlockSpec((T, bp), lambda j: (0, j)), pl.BlockSpec((T, 1), lambda j: (0, 0))],
        out_specs=pl.BlockSpec((1, bp), lambda j: (0, j)),
        out_shape=jax.ShapeDtypeStruct((1, Pn), F32),
    )(soft, r.reshape(T, 1))[0]


def _row_kernel(s_ref, c_ref, o_ref):
    s = s_ref[...]
    o_ref[...] = jnp.sum(s * s * c_ref[...], axis=1, keepdims=True)


def _rowpass(soft, c, bt=64):
    T, Pn = soft.shape
    return pl.pallas_call(
        _row_kernel,
        grid=(T // bt,),
        in_specs=[pl.BlockSpec((bt, Pn), lambda i: (i, 0)), pl.BlockSpec((1, Pn), lambda i: (0, 0))],
        out_specs=pl.BlockSpec((bt, 1), lambda i: (i, 0)),
        out_shape=jax.ShapeDtypeStruct((T, 1), F32),
    )(soft, c.reshape(1, Pn))[:, 0]


def on_device(features, head_weight, prototypes):
    partial_proj = jnp.dot(features, head_weight, preferred_element_type=F32)
    T, E = partial_proj.shape
    nz = SIZES["z"]
    proj_blk = _rs(partial_proj.reshape(nz, T // nz, E), "z", 0)
    projected = _ag(proj_blk, "z").reshape(T, E)
    length = jnp.sqrt(jnp.sum(projected * projected, axis=1, keepdims=True) + 1e-06)
    unit = projected / length
    unit_b = unit.astype(BF16)
    proto_f = prototypes.astype(F32)
    normed = (proto_f / jnp.sqrt(jnp.sum(proto_f * proto_f, axis=0, keepdims=True) + 1e-06)).astype(BF16)
    soft, col0, soft_local = _scores(unit_b, normed)
    kern = soft * soft
    r = None
    soft_total = None
    for step in range(ITERS):
        colpart = col0 if r is None else _colpass(soft, r)
        c = 1.0 / _allsum_dp(colpart)
        rowpart = _rowpass(soft, c)
        if step == 0:
            both = _allsum(jnp.stack([rowpart, soft_local]), "z")
            row, soft_total = both[0], both[1]
        else:
            row = _allsum(rowpart, "z")
        r = 1.0 / row
    plan = kern * c[None, :] * r[:, None]
    probs = soft / soft_total[:, None]
    codes = (PROTOS * plan).astype(BF16)
    tokens_all = 32 * T
    factor = PROTOS / (soft_temp * math.sqrt(tokens_all))
    dscore = ((probs - plan) * factor).astype(BF16)
    half = dscore.shape[1] // 2
    pg = []
    for h in range(2):
        pg_part = lax.dot_general(
            unit_b, dscore[:, h * half:(h + 1) * half], (((0,), (0,)), ((), ())), preferred_element_type=F32
        )
        pg.append(_rs_dp(pg_part, BF16))
    proto_grad = jnp.concatenate(pg, axis=1)
    dunit_part = lax.dot_general(dscore, normed, (((1,), (1,)), ((), ())), preferred_element_type=F32)
    dunit = _allsum(dunit_part, "z", BF16)
    dproj = ((dunit - unit * jnp.sum(unit * dunit, axis=1, keepdims=True)) / length).astype(BF16)
    head_part = lax.dot_general(dproj, features, (((0,), (0,)), ((), ())), preferred_element_type=F32)
    head_grad = _rs_dp(head_part, BF16)
    return (codes, proto_grad, head_grad)


def solution(mesh):
    devs = mesh.devices.reshape(SIZES["y"], SIZES["x"], SIZES["core"], SIZES["z"])
    m4 = Mesh(devs, ("y", "x", "core", "z"))
    in_specs = (P(DP, "z"), P("z", None), P(None, "z"))
    out_specs = (P(DP, "z"), P(DP, "z"), P(DP, "z"))
    return jax.shard_map(on_device, mesh=m4, in_specs=in_specs, out_specs=out_specs, check_vma=False)
```

```python
import math

import jax
import jax.numpy as jnp
from jax import lax
from jax.experimental import pallas as pl
from jax.sharding import Mesh
from jax.sharding import PartitionSpec as P

PROTOS = 32768
ITERS = 3


sink_eps = 0.05
soft_temp = 0.1

DP = ("y", "x", "core")
SIZES = {"y": 4, "x": 4, "core": 2, "z": 4}
F32 = jnp.float32
BF16 = jnp.bfloat16


def _shift(v, ax, k):
    n = SIZES[ax]
    return lax.ppermute(v, ax, [(i, (i + k) % n) for i in range(n)])


def _allsum(v, ax, dt=None):
    sent = v if dt is None else v.astype(dt)
    acc = v
    for k in range(1, SIZES[ax]):
        acc = acc + _shift(sent, ax, k).astype(v.dtype)
    return acc


def _allsum_dp(v):
    for ax in ("core", "x", "y"):
        v = _allsum(v, ax)
    return v


def _rs(a, ax, axis, dt=None):
    n = SIZES[ax]
    i = lax.axis_index(ax)
    acc = lax.dynamic_index_in_dim(a, i, axis, keepdims=False)
    for k in range(1, n):
        blk = lax.dynamic_index_in_dim(a, (i + k) % n, axis, keepdims=False)
        if dt is not None:
            blk = blk.astype(dt)
        acc = acc + _shift(blk, ax, k).astype(a.dtype)
    return acc


def _ag(v, ax):
    n = SIZES[ax]
    i = lax.axis_index(ax)
    parts = [v] + [_shift(v, ax, k) for k in range(1, n)]
    rel = jnp.stack(parts)
    idx = (i - jnp.arange(n)) % n
    return rel[idx]


def _rs_dp(part, dt):
    R, N = part.shape
    a = part.reshape(SIZES["y"], SIZES["x"], SIZES["core"], R // 32, N)
    a = _rs(a, "core", 2, dt)
    a = _rs(a, "x", 1, dt)
    a = _rs(a, "y", 0, dt)
    return a


def _score_kernel(u_ref, n_ref, s_ref, col_ref, rs_ref):
    j = pl.program_id(0)
    sc = jnp.dot(u_ref[...], n_ref[...], preferred_element_type=F32)
    s = jnp.exp(sc * (1.0 / soft_temp))
    s_ref[...] = s
    col_ref[...] = jnp.sum(s * s, axis=0, keepdims=True)

    @pl.when(j == 0)
    def _():
        rs_ref[...] = jnp.zeros_like(rs_ref)

    rs_ref[...] += jnp.sum(s, axis=1, keepdims=True)


def _scores(unit_b, normed, bp=1024):
    T, E = unit_b.shape
    Pn = normed.shape[1]
    soft, col, rs = pl.pallas_call(
        _score_kernel,
        grid=(Pn // bp,),
        in_specs=[pl.BlockSpec((T, E), lambda j: (0, 0)), pl.BlockSpec((E, bp), lambda j: (0, j))],
        out_specs=[
            pl.BlockSpec((T, bp), lambda j: (0, j)),
            pl.BlockSpec((1, bp), lambda j: (0, j)),
            pl.BlockSpec((T, 1), lambda j: (0, 0)),
        ],
        out_shape=[
            jax.ShapeDtypeStruct((T, Pn), F32),
            jax.ShapeDtypeStruct((1, Pn), F32),
            jax.ShapeDtypeStruct((T, 1), F32),
        ],
    )(unit_b, normed)
    return soft, col[0], rs[:, 0]


def _col_kernel(s_ref, r_ref, o_ref):
    s = s_ref[...]
    o_ref[...] = jnp.sum(s * s * r_ref[...], axis=0, keepdims=True)


def _colpass(soft, r, bp=1024):
    T, Pn = soft.shape
    return pl.pallas_call(
        _col_kernel,
        grid=(Pn // bp,),
        in_specs=[pl.BlockSpec((T, bp), lambda j: (0, j)), pl.BlockSpec((T, 1), lambda j: (0, 0))],
        out_specs=pl.BlockSpec((1, bp), lambda j: (0, j)),
        out_shape=jax.ShapeDtypeStruct((1, Pn), F32),
    )(soft, r.reshape(T, 1))[0]


def _row_kernel(s_ref, c_ref, o_ref):
    s = s_ref[...]
    o_ref[...] = jnp.sum(s * s * c_ref[...], axis=1, keepdims=True)


def _rowpass(soft, c, bt=64):
    T, Pn = soft.shape
    return pl.pallas_call(
        _row_kernel,
        grid=(T // bt,),
        in_specs=[pl.BlockSpec((bt, Pn), lambda i: (i, 0)), pl.BlockSpec((1, Pn), lambda i: (0, 0))],
        out_specs=pl.BlockSpec((bt, 1), lambda i: (i, 0)),
        out_shape=jax.ShapeDtypeStruct((T, 1), F32),
    )(soft, c.reshape(1, Pn))[:, 0]


def on_device(features, head_weight, prototypes):
    partial_proj = jnp.dot(features, head_weight, preferred_element_type=F32)
    T, E = partial_proj.shape
    nz = SIZES["z"]
    proj_blk = _rs(partial_proj.reshape(nz, T // nz, E), "z", 0)
    projected = _ag(proj_blk, "z").reshape(T, E)
    length = jnp.sqrt(jnp.sum(projected * projected, axis=1, keepdims=True) + 1e-06)
    unit = projected / length
    unit_b = unit.astype(BF16)
    proto_f = prototypes.astype(F32)
    normed = (proto_f / jnp.sqrt(jnp.sum(proto_f * proto_f, axis=0, keepdims=True) + 1e-06)).astype(BF16)
    soft, col0, soft_local = _scores(unit_b, normed)
    kern = soft * soft
    r = None
    soft_total = None
    for step in range(ITERS):
        colpart = col0 if r is None else _colpass(soft, r)
        c = 1.0 / _allsum_dp(colpart)
        rowpart = _rowpass(soft, c)
        if step == 0:
            both = _allsum(jnp.stack([rowpart, soft_local]), "z")
            row, soft_total = both[0], both[1]
        else:
            row = _allsum(rowpart, "z")
        r = 1.0 / row
    plan = kern * c[None, :] * r[:, None]
    probs = soft / soft_total[:, None]
    codes = (PROTOS * plan).astype(BF16)
    tokens_all = 32 * T
    factor = PROTOS / (soft_temp * math.sqrt(tokens_all))
    dscore = ((probs - plan) * factor).astype(BF16)
    pg_part = lax.dot_general(unit_b, dscore, (((0,), (0,)), ((), ())), preferred_element_type=F32)
    dunit_part = lax.dot_general(dscore, normed, (((1,), (1,)), ((), ())), preferred_element_type=F32)
    dunit = _allsum(dunit_part, "z", BF16)
    dproj = ((dunit - unit * jnp.sum(unit * dunit, axis=1, keepdims=True)) / length).astype(BF16)
    head_part = lax.dot_general(dproj, features, (((0,), (0,)), ((), ())), preferred_element_type=F32)
    Pn = pg_part.shape[1]
    both = _rs_dp(jnp.concatenate([pg_part, head_part], axis=1), BF16)
    return (codes, both[:, :Pn], both[:, Pn:])


def solution(mesh):
    devs = mesh.devices.reshape(SIZES["y"], SIZES["x"], SIZES["core"], SIZES["z"])
    m4 = Mesh(devs, ("y", "x", "core", "z"))
    in_specs = (P(DP, "z"), P("z", None), P(None, "z"))
    out_specs = (P(DP, "z"), P(DP, "z"), P(DP, "z"))
    return jax.shard_map(on_device, mesh=m4, in_specs=in_specs, out_specs=out_specs, check_vma=False)
```

```python
import math

import jax
import jax.numpy as jnp
from jax import lax
from jax.experimental import pallas as pl
from jax.sharding import Mesh

from jax.sharding import PartitionSpec as P

PROTOS = 32768
ITERS = 3


soft_temp = 0.1

DP = ("y", "x", "core")
SIZES = {"y": 4, "x": 4, "core": 2, "z": 4}
F32 = jnp.float32
BF16 = jnp.bfloat16


def _shift(v, ax, k):
    n = SIZES[ax]
    return lax.ppermute(v, ax, [(i, (i + k) % n) for i in range(n)])


def _allsum(v, ax, dt=None):
    sent = v if dt is None else v.astype(dt)
    acc = v
    for k in range(1, SIZES[ax]):
        acc = acc + _shift(sent, ax, k).astype(v.dtype)
    return acc


def _allsum_dp(v):
    for ax in ("core", "x", "y"):
        v = _allsum(v, ax)
    return v


def _rs(a, ax, axis, dt=None):
    n = SIZES[ax]
    i = lax.axis_index(ax)
    acc = lax.dynamic_index_in_dim(a, i, axis, keepdims=False)
    for k in range(1, n):
        blk = lax.dynamic_index_in_dim(a, (i + k) % n, axis, keepdims=False)
        if dt is not None:
            blk = blk.astype(dt)
        acc = acc + _shift(blk, ax, k).astype(a.dtype)
    return acc


def _ag(v, ax):
    n = SIZES[ax]
    i = lax.axis_index(ax)
    parts = [v] + [_shift(v, ax, k) for k in range(1, n)]
    rel = jnp.stack(parts)
    idx = (i - jnp.arange(n)) % n
    return rel[idx]


def _rs_dp(part, dt):
    R, N = part.shape
    a = part.reshape(SIZES["y"], SIZES["x"], SIZES["core"], R // 32, N)
    a = _rs(a, "core", 2, dt)
    a = _rs(a, "x", 1, dt)
    a = _rs(a, "y", 0, dt)
    return a


def _score_kernel(u_ref, n_ref, s_ref, col_ref, rs_ref):
    j = pl.program_id(0)
    sc = jnp.dot(u_ref[...], n_ref[...], preferred_element_type=F32)
    s = jnp.exp(sc * (1.0 / soft_temp))
    s_ref[...] = s
    col_ref[...] = jnp.sum(s * s, axis=0, keepdims=True)

    @pl.when(j == 0)
    def _():
        rs_ref[...] = jnp.zeros_like(rs_ref)

    rs_ref[...] += jnp.sum(s, axis=1, keepdims=True)


def _scores(unit_b, normed, bp=1024):
    T, E = unit_b.shape
    Pn = normed.shape[1]
    soft, col, rs = pl.pallas_call(
        _score_kernel,
        grid=(Pn // bp,),
        in_specs=[pl.BlockSpec((T, E), lambda j: (0, 0)), pl.BlockSpec((E, bp), lambda j: (0, j))],
        out_specs=[
            pl.BlockSpec((T, bp), lambda j: (0, j)),
            pl.BlockSpec((1, bp), lambda j: (0, j)),
            pl.BlockSpec((T, 1), lambda j: (0, 0)),
        ],
        out_shape=[
            jax.ShapeDtypeStruct((T, Pn), F32),
            jax.ShapeDtypeStruct((1, Pn), F32),
            jax.ShapeDtypeStruct((T, 1), F32),
        ],
    )(unit_b, normed)
    return soft, col[0], rs[:, 0]


def _col_kernel(s_ref, r_ref, o_ref):
    s = s_ref[...]
    o_ref[...] = jnp.sum(s * s * r_ref[...], axis=0, keepdims=True)


def _colpass(soft, r, bp=1024):
    T, Pn = soft.shape
    return pl.pallas_call(
        _col_kernel,
        grid=(Pn // bp,),
        in_specs=[pl.BlockSpec((T, bp), lambda j: (0, j)), pl.BlockSpec((T, 1), lambda j: (0, 0))],
        out_specs=pl.BlockSpec((1, bp), lambda j: (0, j)),
        out_shape=jax.ShapeDtypeStruct((1, Pn), F32),
    )(soft, r.reshape(T, 1))[0]


def _row_kernel(s_ref, c_ref, o_ref):
    s = s_ref[...]
    o_ref[...] = jnp.sum(s * s * c_ref[...], axis=1, keepdims=True)


def _rowpass(soft, c, bt=64):
    T, Pn = soft.shape
    return pl.pallas_call(
        _row_kernel,
        grid=(T // bt,),
        in_specs=[pl.BlockSpec((bt, Pn), lambda i: (i, 0)), pl.BlockSpec((1, Pn), lambda i: (0, 0))],
        out_specs=pl.BlockSpec((bt, 1), lambda i: (i, 0)),
        out_shape=jax.ShapeDtypeStruct((T, 1), F32),
    )(soft, c.reshape(1, Pn))[:, 0]


def on_device(features, head_weight, prototypes):
    partial_proj = jnp.dot(features, head_weight, preferred_element_type=F32)
    T, E = partial_proj.shape
    nz = SIZES["z"]
    proj_blk = _rs(partial_proj.reshape(nz, T // nz, E), "z", 0)
    projected = _ag(proj_blk, "z").reshape(T, E)
    length = jnp.sqrt(jnp.sum(projected * projected, axis=1, keepdims=True) + 1e-06)
    unit = projected / length
    unit_b = unit.astype(BF16)
    proto_f = prototypes.astype(F32)
    normed = (proto_f / jnp.sqrt(jnp.sum(proto_f * proto_f, axis=0, keepdims=True) + 1e-06)).astype(BF16)
    soft, col0, soft_local = _scores(unit_b, normed)
    kern = soft * soft
    r = None
    soft_total = None
    for step in range(ITERS):
        colpart = col0 if r is None else _colpass(soft, r)
        c = 1.0 / _allsum_dp(colpart)
        rowpart = _rowpass(soft, c)
        if step == 0:
            both = _allsum(jnp.stack([rowpart, soft_local]), "z")
            row, soft_total = both[0], both[1]
        else:
            row = _allsum(rowpart, "z")
        r = 1.0 / row
    plan = kern * c[None, :] * r[:, None]
    probs = soft / soft_total[:, None]
    codes = (PROTOS * plan).astype(BF16)
    tokens_all = 32 * T
    factor = PROTOS / (soft_temp * math.sqrt(tokens_all))
    dscore = ((probs - plan) * factor).astype(BF16)
    pg_part = lax.dot_general(unit_b, dscore, (((0,), (0,)), ((), ())), preferred_element_type=F32)
    R, N = pg_part.shape
    a = pg_part.reshape(SIZES["y"], SIZES["x"], SIZES["core"], R // 32, N)
    a = _rs(a, "core", 2, BF16)
    dunit_part = lax.dot_general(dscore, normed, (((1,), (1,)), ((), ())), preferred_element_type=F32)
    a = _rs(a, "x", 1, BF16)
    dunit = _allsum(dunit_part, "z", BF16)
    dproj = ((dunit - unit * jnp.sum(unit * dunit, axis=1, keepdims=True)) / length).astype(BF16)
    head_part = lax.dot_general(dproj, features, (((0,), (0,)), ((), ())), preferred_element_type=F32)
    head_grad = _rs_dp(head_part, BF16)
    proto_grad = _rs(a, "y", 0, BF16)
    return (codes, proto_grad, head_grad)


def solution(mesh):
    devs = mesh.devices.reshape(SIZES["y"], SIZES["x"], SIZES["core"], SIZES["z"])
    m4 = Mesh(devs, ("y", "x", "core", "z"))
    in_specs = (P(DP, "z"), P("z", None), P(None, "z"))
    out_specs = (P(DP, "z"), P(DP, "z"), P(DP, "z"))

    return jax.shard_map(on_device, mesh=m4, in_specs=in_specs, out_specs=out_specs, check_vma=False)
```

```python
import math

import jax
import jax.numpy as jnp
from jax import lax
from jax.experimental import pallas as pl
from jax.sharding import Mesh
from jax.sharding import PartitionSpec as P

PROTOS = 32768
ITERS = 3


soft_temp = 0.1

DP = ("y", "x", "core")
SIZES = {"y": 4, "x": 4, "core": 2, "z": 4}
F32 = jnp.float32
BF16 = jnp.bfloat16


def _shift(v, ax, k):
    n = SIZES[ax]
    return lax.ppermute(v, ax, [(i, (i + k) % n) for i in range(n)])


def _allsum(v, ax, dt=None):
    sent = v if dt is None else v.astype(dt)
    acc = v
    for k in range(1, SIZES[ax]):
        acc = acc + _shift(sent, ax, k).astype(v.dtype)
    return acc


def _allsum_dp(v):
    for ax in ("core", "x", "y"):
        v = _allsum(v, ax)
    return v


def _rs(a, ax, axis, dt=None):
    n = SIZES[ax]
    i = lax.axis_index(ax)
    acc = lax.dynamic_index_in_dim(a, i, axis, keepdims=False)
    for k in range(1, n):
        blk = lax.dynamic_index_in_dim(a, (i + k) % n, axis, keepdims=False)
        if dt is not None:
            blk = blk.astype(dt)
        acc = acc + _shift(blk, ax, k).astype(a.dtype)
    return acc


def _ag(v, ax):
    n = SIZES[ax]
    i = lax.axis_index(ax)
    parts = [v] + [_shift(v, ax, k) for k in range(1, n)]
    rel = jnp.stack(parts)
    idx = (i - jnp.arange(n)) % n
    return rel[idx]


def _rs_dp(part, dt):
    R, N = part.shape
    a = part.reshape(SIZES["y"], SIZES["x"], SIZES["core"], R // 32, N)
    a = _rs(a, "core", 2, dt)
    a = _rs(a, "x", 1, dt)
    a = _rs(a, "y", 0, dt)
    return a


def _score_kernel(u_ref, n_ref, s_ref, k_ref, col_ref, rs_ref):
    j = pl.program_id(0)
    sc = jnp.dot(u_ref[...], n_ref[...], preferred_element_type=F32)
    s = jnp.exp(sc * (1.0 / soft_temp))
    s_ref[...] = s
    k = s * s
    k_ref[...] = k.astype(BF16)
    col_ref[...] = jnp.sum(k, axis=0, keepdims=True)

    @pl.when(j == 0)
    def _():
        rs_ref[...] = jnp.zeros_like(rs_ref)

    rs_ref[...] += jnp.sum(s, axis=1, keepdims=True)


def _scores(unit_b, normed, bp=1024):
    T, E = unit_b.shape
    Pn = normed.shape[1]
    soft, kb, col, rs = pl.pallas_call(
        _score_kernel,
        grid=(Pn // bp,),
        in_specs=[pl.BlockSpec((T, E), lambda j: (0, 0)), pl.BlockSpec((E, bp), lambda j: (0, j))],
        out_specs=[
            pl.BlockSpec((T, bp), lambda j: (0, j)),
            pl.BlockSpec((T, bp), lambda j: (0, j)),
            pl.BlockSpec((1, bp), lambda j: (0, j)),
            pl.BlockSpec((T, 1), lambda j: (0, 0)),
        ],
        out_shape=[
            jax.ShapeDtypeStruct((T, Pn), F32),
            jax.ShapeDtypeStruct((T, Pn), BF16),
            jax.ShapeDtypeStruct((1, Pn), F32),
            jax.ShapeDtypeStruct((T, 1), F32),
        ],
    )(unit_b, normed)
    return soft, kb, col[0], rs[:, 0]


def _col_kernel(k_ref, r_ref, o_ref):
    k = k_ref[...].astype(F32)
    o_ref[...] = jnp.sum(k * r_ref[...], axis=0, keepdims=True)


def _colpass(soft, r, bp=1024):
    T, Pn = soft.shape
    return pl.pallas_call(
        _col_kernel,
        grid=(Pn // bp,),
        in_specs=[pl.BlockSpec((T, bp), lambda j: (0, j)), pl.BlockSpec((T, 1), lambda j: (0, 0))],
        out_specs=pl.BlockSpec((1, bp), lambda j: (0, j)),
        out_shape=jax.ShapeDtypeStruct((1, Pn), F32),
    )(soft, r.reshape(T, 1))[0]


def _row_kernel(k_ref, c_ref, o_ref):
    k = k_ref[...].astype(F32)
    o_ref[...] = jnp.sum(k * c_ref[...], axis=1, keepdims=True)


def _rowpass(soft, c, bt=64):
    T, Pn = soft.shape
    return pl.pallas_call(
        _row_kernel,
        grid=(T // bt,),
        in_specs=[pl.BlockSpec((bt, Pn), lambda i: (i, 0)), pl.BlockSpec((1, Pn), lambda i: (0, 0))],
        out_specs=pl.BlockSpec((bt, 1), lambda i: (i, 0)),
        out_shape=jax.ShapeDtypeStruct((T, 1), F32),
    )(soft, c.reshape(1, Pn))[:, 0]


def on_device(features, head_weight, prototypes):
    partial_proj = jnp.dot(features, head_weight, preferred_element_type=F32)
    T, E = partial_proj.shape
    nz = SIZES["z"]
    proj_blk = _rs(partial_proj.reshape(nz, T // nz, E), "z", 0)
    projected = _ag(proj_blk, "z").reshape(T, E)
    length = jnp.sqrt(jnp.sum(projected * projected, axis=1, keepdims=True) + 1e-06)
    unit = projected / length
    unit_b = unit.astype(BF16)
    proto_f = prototypes.astype(F32)
    normed = (proto_f / jnp.sqrt(jnp.sum(proto_f * proto_f, axis=0, keepdims=True) + 1e-06)).astype(BF16)
    soft, kern_b, col0, soft_local = _scores(unit_b, normed)
    kern = soft * soft
    r = None
    soft_total = None
    for step in range(ITERS):
        colpart = col0 if r is None else _colpass(kern_b, r)
        c = 1.0 / _allsum_dp(colpart)
        rowpart = _rowpass(kern_b, c)
        if step == 0:
            both = _allsum(jnp.stack([rowpart, soft_local]), "z")
            row, soft_total = both[0], both[1]
        else:
            row = _allsum(rowpart, "z")
        r = 1.0 / row
    plan = kern * c[None, :] * r[:, None]
    probs = soft / soft_total[:, None]
    codes = (PROTOS * plan).astype(BF16)
    tokens_all = 32 * T
    factor = PROTOS / (soft_temp * math.sqrt(tokens_all))
    dscore = ((probs - plan) * factor).astype(BF16)
    pg_part = lax.dot_general(unit_b, dscore, (((0,), (0,)), ((), ())), preferred_element_type=F32)
    R, N = pg_part.shape
    a = pg_part.reshape(SIZES["y"], SIZES["x"], SIZES["core"], R // 32, N)
    a = _rs(a, "core", 2, BF16)
    dunit_part = lax.dot_general(dscore, normed, (((1,), (1,)), ((), ())), preferred_element_type=F32)
    a = _rs(a, "x", 1, BF16)
    dunit = _allsum(dunit_part, "z", BF16)
    dproj = ((dunit - unit * jnp.sum(unit * dunit, axis=1, keepdims=True)) / length).astype(BF16)
    head_part = lax.dot_general(dproj, features, (((0,), (0,)), ((), ())), preferred_element_type=F32)
    head_grad = _rs_dp(head_part, BF16)
    proto_grad = _rs(a, "y", 0, BF16)
    return (codes, proto_grad, head_grad)


def solution(mesh):
    devs = mesh.devices.reshape(SIZES["y"], SIZES["x"], SIZES["core"], SIZES["z"])
    m4 = Mesh(devs, ("y", "x", "core", "z"))
    in_specs = (P(DP, "z"), P("z", None), P(None, "z"))
    out_specs = (P(DP, "z"), P(DP, "z"), P(DP, "z"))

    return jax.shard_map(on_device, mesh=m4, in_specs=in_specs, out_specs=out_specs, check_vma=False)
```

```python
import math

import jax
import jax.numpy as jnp
from jax import lax
from jax.experimental import pallas as pl
from jax.experimental.pallas import tpu as pltpu
from jax.sharding import Mesh
from jax.sharding import PartitionSpec as P

PROTOS = 32768
ITERS = 3


soft_temp = 0.1

DP = ("y", "x", "core")
SIZES = {"y": 4, "x": 4, "core": 2, "z": 4}
F32 = jnp.float32
BF16 = jnp.bfloat16


def _shift(v, ax, k):
    n = SIZES[ax]
    return lax.ppermute(v, ax, [(i, (i + k) % n) for i in range(n)])


def _allsum(v, ax, dt=None):
    sent = v if dt is None else v.astype(dt)
    acc = v
    for k in range(1, SIZES[ax]):
        acc = acc + _shift(sent, ax, k).astype(v.dtype)
    return acc


def _allsum_dp(v):
    for ax in ("core", "x", "y"):
        v = _allsum(v, ax)
    return v


def _rs(a, ax, axis, dt=None):
    n = SIZES[ax]
    i = lax.axis_index(ax)
    acc = lax.dynamic_index_in_dim(a, i, axis, keepdims=False)
    for k in range(1, n):
        blk = lax.dynamic_index_in_dim(a, (i + k) % n, axis, keepdims=False)
        if dt is not None:
            blk = blk.astype(dt)
        acc = acc + _shift(blk, ax, k).astype(a.dtype)
    return acc


def _ag(v, ax):
    n = SIZES[ax]
    i = lax.axis_index(ax)
    parts = [v] + [_shift(v, ax, k) for k in range(1, n)]
    rel = jnp.stack(parts)
    idx = (i - jnp.arange(n)) % n
    return rel[idx]


def _rs_dp(part, dt):
    R, N = part.shape
    a = part.reshape(SIZES["y"], SIZES["x"], SIZES["core"], R // 32, N)
    a = _rs(a, "core", 2, dt)
    a = _rs(a, "x", 1, dt)
    a = _rs(a, "y", 0, dt)
    return a


def _score_kernel(u_ref, n_ref, s_ref, k_ref, col_ref, rs_ref):
    j = pl.program_id(0)
    sc = jnp.dot(u_ref[...], n_ref[...], preferred_element_type=F32)
    s = jnp.exp(sc * (1.0 / soft_temp))
    s_ref[...] = s
    k = s * s
    k_ref[:, pl.ds(pl.multiple_of(j * s.shape[1], s.shape[1]), s.shape[1])] = k.astype(BF16)
    col_ref[...] = jnp.sum(k, axis=0, keepdims=True)

    @pl.when(j == 0)
    def _():
        rs_ref[...] = jnp.zeros_like(rs_ref)

    rs_ref[...] += jnp.sum(s, axis=1, keepdims=True)


def _scores(unit_b, normed, bp=1024):
    T, E = unit_b.shape
    Pn = normed.shape[1]
    soft, kb, col, rs = pl.pallas_call(
        _score_kernel,
        grid=(Pn // bp,),
        in_specs=[pl.BlockSpec((T, E), lambda j: (0, 0)), pl.BlockSpec((E, bp), lambda j: (0, j))],
        out_specs=[
            pl.BlockSpec((T, bp), lambda j: (0, j)),
            pl.BlockSpec(memory_space=pltpu.VMEM),
            pl.BlockSpec((1, bp), lambda j: (0, j)),
            pl.BlockSpec((T, 1), lambda j: (0, 0)),
        ],
        out_shape=[
            jax.ShapeDtypeStruct((T, Pn), F32),
            jax.ShapeDtypeStruct((T, Pn), BF16),
            jax.ShapeDtypeStruct((1, Pn), F32),
            jax.ShapeDtypeStruct((T, 1), F32),
        ],
    )(unit_b, normed)
    return soft, kb, col[0], rs[:, 0]


def _col_kernel(k_ref, r_ref, o_ref):
    _, Pn = k_ref.shape
    w = 512

    def body(j, carry):
        sl = pl.ds(pl.multiple_of(j * w, w), w)
        k = k_ref[:, sl].astype(F32)
        o_ref[:, sl] = jnp.sum(k * r_ref[...], axis=0, keepdims=True)
        return carry

    lax.fori_loop(0, Pn // w, body, 0)


_VMEM = pl.BlockSpec(memory_space=pltpu.VMEM)


def _colpass(kern_b, r):
    T, Pn = kern_b.shape
    return pl.pallas_call(
        _col_kernel,
        in_specs=[_VMEM, _VMEM],
        out_specs=_VMEM,
        out_shape=jax.ShapeDtypeStruct((1, Pn), F32),
    )(kern_b, r.reshape(T, 1))[0]


def _row_kernel(k_ref, c_ref, o_ref):
    T, _ = k_ref.shape
    h = 32

    def body(i, carry):
        sl = pl.ds(pl.multiple_of(i * h, h), h)
        k = k_ref[sl, :].astype(F32)
        o_ref[sl, :] = jnp.sum(k * c_ref[...], axis=1, keepdims=True)
        return carry

    lax.fori_loop(0, T // h, body, 0)


def _rowpass(kern_b, c):
    T, Pn = kern_b.shape
    return pl.pallas_call(
        _row_kernel,
        in_specs=[_VMEM, _VMEM],
        out_specs=_VMEM,
        out_shape=jax.ShapeDtypeStruct((T, 1), F32),
    )(kern_b, c.reshape(1, Pn))[:, 0]


def on_device(features, head_weight, prototypes):
    partial_proj = jnp.dot(features, head_weight, preferred_element_type=F32)
    T, E = partial_proj.shape
    nz = SIZES["z"]
    proj_blk = _rs(partial_proj.reshape(nz, T // nz, E), "z", 0)
    projected = _ag(proj_blk, "z").reshape(T, E)
    length = jnp.sqrt(jnp.sum(projected * projected, axis=1, keepdims=True) + 1e-06)
    unit = projected / length
    unit_b = unit.astype(BF16)
    proto_f = prototypes.astype(F32)
    normed = (proto_f / jnp.sqrt(jnp.sum(proto_f * proto_f, axis=0, keepdims=True) + 1e-06)).astype(BF16)
    soft, kern_b, col0, soft_local = _scores(unit_b, normed)
    kern = soft * soft
    r = None
    soft_total = None
    for step in range(ITERS):
        colpart = col0 if r is None else _colpass(kern_b, r)
        c = 1.0 / _allsum_dp(colpart)
        rowpart = _rowpass(kern_b, c)
        if step == 0:
            both = _allsum(jnp.stack([rowpart, soft_local]), "z")
            row, soft_total = both[0], both[1]
        else:
            row = _allsum(rowpart, "z")
        r = 1.0 / row
    plan = kern * c[None, :] * r[:, None]
    probs = soft / soft_total[:, None]
    codes = (PROTOS * plan).astype(BF16)
    tokens_all = 32 * T
    factor = PROTOS / (soft_temp * math.sqrt(tokens_all))
    dscore = ((probs - plan) * factor).astype(BF16)
    pg_part = lax.dot_general(unit_b, dscore, (((0,), (0,)), ((), ())), preferred_element_type=F32)
    R, N = pg_part.shape
    a = pg_part.reshape(SIZES["y"], SIZES["x"], SIZES["core"], R // 32, N)
    a = _rs(a, "core", 2, BF16)
    dunit_part = lax.dot_general(dscore, normed, (((1,), (1,)), ((), ())), preferred_element_type=F32)
    a = _rs(a, "x", 1, BF16)
    dunit = _allsum(dunit_part, "z", BF16)
    dproj = ((dunit - unit * jnp.sum(unit * dunit, axis=1, keepdims=True)) / length).astype(BF16)
    head_part = lax.dot_general(dproj, features, (((0,), (0,)), ((), ())), preferred_element_type=F32)
    head_grad = _rs_dp(head_part, BF16)
    proto_grad = _rs(a, "y", 0, BF16)
    return (codes, proto_grad, head_grad)


def solution(mesh):
    devs = mesh.devices.reshape(SIZES["y"], SIZES["x"], SIZES["core"], SIZES["z"])
    m4 = Mesh(devs, ("y", "x", "core", "z"))
    in_specs = (P(DP, "z"), P("z", None), P(None, "z"))
    out_specs = (P(DP, "z"), P(DP, "z"), P(DP, "z"))

    return jax.shard_map(on_device, mesh=m4, in_specs=in_specs, out_specs=out_specs, check_vma=False)
```

```python
import math

import jax
import jax.numpy as jnp
from jax import lax
from jax.experimental import pallas as pl
from jax.experimental.pallas import tpu as pltpu
from jax.sharding import Mesh
from jax.sharding import PartitionSpec as P

PROTOS = 32768
ITERS = 3


soft_temp = 0.1

DP = ("y", "x", "core")
SIZES = {"y": 4, "x": 4, "core": 2, "z": 4}
F32 = jnp.float32
BF16 = jnp.bfloat16


def _shift(v, ax, k):
    n = SIZES[ax]
    return lax.ppermute(v, ax, [(i, (i + k) % n) for i in range(n)])


def _allsum(v, ax, dt=None):
    sent = v if dt is None else v.astype(dt)
    acc = v
    for k in range(1, SIZES[ax]):
        acc = acc + _shift(sent, ax, k).astype(v.dtype)
    return acc


def _allsum_dp(v):
    for ax in ("core", "x", "y"):
        v = _allsum(v, ax)
    return v


def _rs(a, ax, axis, dt=None):
    n = SIZES[ax]
    i = lax.axis_index(ax)
    acc = lax.dynamic_index_in_dim(a, i, axis, keepdims=False)
    for k in range(1, n):
        blk = lax.dynamic_index_in_dim(a, (i + k) % n, axis, keepdims=False)
        if dt is not None:
            blk = blk.astype(dt)
        acc = acc + _shift(blk, ax, k).astype(a.dtype)
    return acc


def _ag(v, ax):
    n = SIZES[ax]
    i = lax.axis_index(ax)
    parts = [v] + [_shift(v, ax, k) for k in range(1, n)]
    rel = jnp.stack(parts)
    idx = (i - jnp.arange(n)) % n
    return rel[idx]


def _rs_dp(part, dt):
    R, N = part.shape
    a = part.reshape(SIZES["y"], SIZES["x"], SIZES["core"], R // 32, N)
    a = _rs(a, "core", 2, dt)
    a = _rs(a, "x", 1, dt)
    a = _rs(a, "y", 0, dt)
    return a


def _score_kernel(u_ref, n_ref, s_ref, k_ref, col_ref, rs_ref):
    j = pl.program_id(0)
    sc = jnp.dot(u_ref[...], n_ref[...], preferred_element_type=F32)
    s = jnp.exp(sc * (1.0 / soft_temp))
    s_ref[...] = s
    k = s * s
    k_ref[:, pl.ds(pl.multiple_of(j * s.shape[1], s.shape[1]), s.shape[1])] = k.astype(BF16)
    col_ref[...] = jnp.sum(k, axis=0, keepdims=True)

    @pl.when(j == 0)
    def _():
        rs_ref[...] = jnp.zeros_like(rs_ref)

    rs_ref[...] += jnp.sum(s, axis=1, keepdims=True)


def _scores(unit_b, normed, bp=1024):
    T, E = unit_b.shape
    Pn = normed.shape[1]
    soft, kb, col, rs = pl.pallas_call(
        _score_kernel,
        grid=(Pn // bp,),
        in_specs=[pl.BlockSpec((T, E), lambda j: (0, 0)), pl.BlockSpec((E, bp), lambda j: (0, j))],
        out_specs=[
            pl.BlockSpec((T, bp), lambda j: (0, j)),
            pl.BlockSpec(memory_space=pltpu.VMEM),
            pl.BlockSpec((1, bp), lambda j: (0, j)),
            pl.BlockSpec((T, 1), lambda j: (0, 0)),
        ],
        out_shape=[
            jax.ShapeDtypeStruct((T, Pn), F32),
            jax.ShapeDtypeStruct((T, Pn), BF16),
            jax.ShapeDtypeStruct((1, Pn), F32),
            jax.ShapeDtypeStruct((T, 1), F32),
        ],
    )(unit_b, normed)
    return soft, kb, col[0], rs[:, 0]


def _split(v):
    hi = v.astype(BF16)
    lo = (v - hi.astype(F32)).astype(BF16)
    return jnp.stack([hi, lo])


def _colpass(kern_b, r):
    out = jnp.dot(_split(r), kern_b, preferred_element_type=F32)
    return out[0] + out[1]


def _rowpass(kern_b, c):
    out = jnp.dot(kern_b, _split(c).T, preferred_element_type=F32)
    return out[:, 0] + out[:, 1]


def on_device(features, head_weight, prototypes):
    partial_proj = jnp.dot(features, head_weight, preferred_element_type=F32)
    T, E = partial_proj.shape
    nz = SIZES["z"]
    proj_blk = _rs(partial_proj.reshape(nz, T // nz, E), "z", 0)
    projected = _ag(proj_blk, "z").reshape(T, E)
    length = jnp.sqrt(jnp.sum(projected * projected, axis=1, keepdims=True) + 1e-06)
    unit = projected / length
    unit_b = unit.astype(BF16)
    proto_f = prototypes.astype(F32)
    normed = (proto_f / jnp.sqrt(jnp.sum(proto_f * proto_f, axis=0, keepdims=True) + 1e-06)).astype(BF16)
    soft, kern_b, col0, soft_local = _scores(unit_b, normed)
    kern = soft * soft
    r = None
    soft_total = None
    for step in range(ITERS):
        colpart = col0 if r is None else _colpass(kern_b, r)
        c = 1.0 / _allsum_dp(colpart)
        rowpart = _rowpass(kern_b, c)
        if step == 0:
            both = _allsum(jnp.stack([rowpart, soft_local]), "z")
            row, soft_total = both[0], both[1]
        else:
            row = _allsum(rowpart, "z")
        r = 1.0 / row
    plan = kern * c[None, :] * r[:, None]
    probs = soft / soft_total[:, None]
    codes = (PROTOS * plan).astype(BF16)
    tokens_all = 32 * T
    factor = PROTOS / (soft_temp * math.sqrt(tokens_all))
    dscore = ((probs - plan) * factor).astype(BF16)
    pg_part = lax.dot_general(unit_b, dscore, (((0,), (0,)), ((), ())), preferred_element_type=F32)
    R, N = pg_part.shape
    a = pg_part.reshape(SIZES["y"], SIZES["x"], SIZES["core"], R // 32, N)
    a = _rs(a, "core", 2, BF16)
    dunit_part = lax.dot_general(dscore, normed, (((1,), (1,)), ((), ())), preferred_element_type=F32)
    a = _rs(a, "x", 1, BF16)
    dunit = _allsum(dunit_part, "z", BF16)
    dproj = ((dunit - unit * jnp.sum(unit * dunit, axis=1, keepdims=True)) / length).astype(BF16)
    head_part = lax.dot_general(dproj, features, (((0,), (0,)), ((), ())), preferred_element_type=F32)
    head_grad = _rs_dp(head_part, BF16)
    proto_grad = _rs(a, "y", 0, BF16)
    return (codes, proto_grad, head_grad)


def solution(mesh):
    devs = mesh.devices.reshape(SIZES["y"], SIZES["x"], SIZES["core"], SIZES["z"])
    m4 = Mesh(devs, ("y", "x", "core", "z"))
    in_specs = (P(DP, "z"), P("z", None), P(None, "z"))
    out_specs = (P(DP, "z"), P(DP, "z"), P(DP, "z"))

    return jax.shard_map(on_device, mesh=m4, in_specs=in_specs, out_specs=out_specs, check_vma=False)
```

```python
import functools
import math

import jax
import jax.numpy as jnp
from jax import lax
from jax.experimental import pallas as pl
from jax.experimental.pallas import tpu as pltpu
from jax.sharding import Mesh
from jax.sharding import PartitionSpec as P

PROTOS = 32768
ITERS = 3


soft_temp = 0.1

DP = ("y", "x", "core")
SIZES = {"y": 4, "x": 4, "core": 2, "z": 4}
F32 = jnp.float32
BF16 = jnp.bfloat16


def _shift(v, ax, k):
    n = SIZES[ax]
    return lax.ppermute(v, ax, [(i, (i + k) % n) for i in range(n)])


def _allsum(v, ax, dt=None):
    sent = v if dt is None else v.astype(dt)
    acc = v
    for k in range(1, SIZES[ax]):
        acc = acc + _shift(sent, ax, k).astype(v.dtype)
    return acc


def _allsum_dp(v):
    for ax in ("core", "x", "y"):
        v = _allsum(v, ax)
    return v


def _rs(a, ax, axis, dt=None):
    n = SIZES[ax]
    i = lax.axis_index(ax)
    acc = lax.dynamic_index_in_dim(a, i, axis, keepdims=False)
    for k in range(1, n):
        blk = lax.dynamic_index_in_dim(a, (i + k) % n, axis, keepdims=False)
        if dt is not None:
            blk = blk.astype(dt)
        acc = acc + _shift(blk, ax, k).astype(a.dtype)
    return acc


def _ag(v, ax):
    n = SIZES[ax]
    i = lax.axis_index(ax)
    parts = [v] + [_shift(v, ax, k) for k in range(1, n)]
    rel = jnp.stack(parts)
    idx = (i - jnp.arange(n)) % n
    return rel[idx]


def _rs_dp(part, dt):
    R, N = part.shape
    a = part.reshape(SIZES["y"], SIZES["x"], SIZES["core"], R // 32, N)
    a = _rs(a, "core", 2, dt)
    a = _rs(a, "x", 1, dt)
    a = _rs(a, "y", 0, dt)
    return a


def _soft(u_ref, n_ref):
    sc = jnp.dot(u_ref[...], n_ref[...], preferred_element_type=F32)
    return jnp.exp(sc * (1.0 / soft_temp))


def _score_kernel(u_ref, n_ref, k_ref, col_ref, rs_ref):
    j = pl.program_id(0)
    s = _soft(u_ref, n_ref)
    k = s * s
    k_ref[:, pl.ds(pl.multiple_of(j * s.shape[1], s.shape[1]), s.shape[1])] = k.astype(BF16)
    col_ref[...] = jnp.sum(k, axis=0, keepdims=True)

    @pl.when(j == 0)
    def _():
        rs_ref[...] = jnp.zeros_like(rs_ref)

    rs_ref[...] += jnp.sum(s, axis=1, keepdims=True)


def _scores(unit_b, normed, bp=1024):
    T, E = unit_b.shape
    Pn = normed.shape[1]
    kb, col, rs = pl.pallas_call(
        _score_kernel,
        grid=(Pn // bp,),
        in_specs=[pl.BlockSpec((T, E), lambda j: (0, 0)), pl.BlockSpec((E, bp), lambda j: (0, j))],
        out_specs=[
            pl.BlockSpec(memory_space=pltpu.VMEM),
            pl.BlockSpec((1, bp), lambda j: (0, j)),
            pl.BlockSpec((T, 1), lambda j: (0, 0)),
        ],
        out_shape=[
            jax.ShapeDtypeStruct((T, Pn), BF16),
            jax.ShapeDtypeStruct((1, Pn), F32),
            jax.ShapeDtypeStruct((T, 1), F32),
        ],
    )(unit_b, normed)
    return kb, col[0], rs[:, 0]


def _final_kernel(u_ref, ut_ref, n_ref, c_ref, r_ref, si_ref, codes_ref, pg_ref, du_ref, *, factor):
    j = pl.program_id(0)
    s = _soft(u_ref, n_ref)
    plan = (s * s) * c_ref[...] * r_ref[...]
    probs = s * si_ref[...]
    codes_ref[...] = (PROTOS * plan).astype(BF16)
    d = ((probs - plan) * factor).astype(BF16)
    pg_ref[...] = jnp.dot(ut_ref[...], d, preferred_element_type=F32)

    @pl.when(j == 0)
    def _():
        du_ref[...] = jnp.zeros_like(du_ref)

    du_ref[...] += lax.dot_general(d, n_ref[...], (((1,), (1,)), ((), ())), preferred_element_type=F32)


def _final(unit_b, normed, c, r, soft_inv, factor, bp=512):
    T, E = unit_b.shape
    Pn = normed.shape[1]
    return pl.pallas_call(
        functools.partial(_final_kernel, factor=factor),
        grid=(Pn // bp,),
        in_specs=[
            pl.BlockSpec((T, E), lambda j: (0, 0)),
            pl.BlockSpec((E, T), lambda j: (0, 0)),
            pl.BlockSpec((E, bp), lambda j: (0, j)),
            pl.BlockSpec((1, bp), lambda j: (0, j)),
            pl.BlockSpec((T, 1), lambda j: (0, 0)),
            pl.BlockSpec((T, 1), lambda j: (0, 0)),
        ],
        out_specs=[
            pl.BlockSpec((T, bp), lambda j: (0, j)),
            pl.BlockSpec((E, bp), lambda j: (0, j)),
            pl.BlockSpec((T, E), lambda j: (0, 0)),
        ],
        out_shape=[
            jax.ShapeDtypeStruct((T, Pn), BF16),
            jax.ShapeDtypeStruct((E, Pn), F32),
            jax.ShapeDtypeStruct((T, E), F32),
        ],
    )(unit_b, unit_b.T, normed, c.reshape(1, Pn), r.reshape(T, 1), soft_inv.reshape(T, 1))


def _split(v):
    hi = v.astype(BF16)
    lo = (v - hi.astype(F32)).astype(BF16)
    return jnp.stack([hi, lo])


def _colpass(kern_b, r):
    out = jnp.dot(_split(r), kern_b, preferred_element_type=F32)
    return out[0] + out[1]


def _rowpass(kern_b, c):
    out = jnp.dot(kern_b, _split(c).T, preferred_element_type=F32)
    return out[:, 0] + out[:, 1]


def on_device(features, head_weight, prototypes):
    partial_proj = jnp.dot(features, head_weight, preferred_element_type=F32)
    T, E = partial_proj.shape
    nz = SIZES["z"]
    proj_blk = _rs(partial_proj.reshape(nz, T // nz, E), "z", 0)
    projected = _ag(proj_blk, "z").reshape(T, E)
    length = jnp.sqrt(jnp.sum(projected * projected, axis=1, keepdims=True) + 1e-06)
    unit = projected / length
    unit_b = unit.astype(BF16)
    proto_f = prototypes.astype(F32)
    normed = (proto_f / jnp.sqrt(jnp.sum(proto_f * proto_f, axis=0, keepdims=True) + 1e-06)).astype(BF16)
    kern_b, col0, soft_local = _scores(unit_b, normed)
    r = None
    soft_total = None
    for step in range(ITERS):
        colpart = col0 if r is None else _colpass(kern_b, r)
        c = 1.0 / _allsum_dp(colpart)
        rowpart = _rowpass(kern_b, c)
        if step == 0:
            both = _allsum(jnp.stack([rowpart, soft_local]), "z")
            row, soft_total = both[0], both[1]
        else:
            row = _allsum(rowpart, "z")
        r = 1.0 / row
    tokens_all = 32 * T
    factor = PROTOS / (soft_temp * math.sqrt(tokens_all))
    codes, pg_part, dunit_part = _final(unit_b, normed, c, r, 1.0 / soft_total, factor)
    R, N = pg_part.shape
    a = pg_part.reshape(SIZES["y"], SIZES["x"], SIZES["core"], R // 32, N)
    a = _rs(a, "core", 2, BF16)
    a = _rs(a, "x", 1, BF16)
    dunit = _allsum(dunit_part, "z", BF16)
    dproj = ((dunit - unit * jnp.sum(unit * dunit, axis=1, keepdims=True)) / length).astype(BF16)
    head_part = lax.dot_general(dproj, features, (((0,), (0,)), ((), ())), preferred_element_type=F32)
    head_grad = _rs_dp(head_part, BF16)
    proto_grad = _rs(a, "y", 0, BF16)
    return (codes, proto_grad, head_grad)


def solution(mesh):
    devs = mesh.devices.reshape(SIZES["y"], SIZES["x"], SIZES["core"], SIZES["z"])
    m4 = Mesh(devs, ("y", "x", "core", "z"))
    in_specs = (P(DP, "z"), P("z", None), P(None, "z"))
    out_specs = (P(DP, "z"), P(DP, "z"), P(DP, "z"))

    return jax.shard_map(on_device, mesh=m4, in_specs=in_specs, out_specs=out_specs, check_vma=False)
```

```python
import math

import jax
import jax.numpy as jnp
from jax import lax
from jax.experimental import pallas as pl
from jax.experimental.pallas import tpu as pltpu
from jax.sharding import Mesh
from jax.sharding import PartitionSpec as P

PROTOS = 32768
ITERS = 3


soft_temp = 0.1

DP = ("y", "x", "core")
SIZES = {"y": 4, "x": 4, "core": 2, "z": 4}
F32 = jnp.float32
BF16 = jnp.bfloat16


def _shift(v, ax, k):
    n = SIZES[ax]
    return lax.ppermute(v, ax, [(i, (i + k) % n) for i in range(n)])


def _allsum(v, ax, dt=None):
    sent = v if dt is None else v.astype(dt)
    acc = v
    for k in range(1, SIZES[ax]):
        acc = acc + _shift(sent, ax, k).astype(v.dtype)
    return acc


def _allsum_dp(v):
    for ax in ("core", "x", "y"):
        v = _allsum(v, ax)
    return v


def _rs(a, ax, axis, dt=None):
    n = SIZES[ax]
    i = lax.axis_index(ax)
    acc = lax.dynamic_index_in_dim(a, i, axis, keepdims=False)
    for k in range(1, n):
        blk = lax.dynamic_index_in_dim(a, (i + k) % n, axis, keepdims=False)
        if dt is not None:
            blk = blk.astype(dt)
        acc = acc + _shift(blk, ax, k).astype(a.dtype)
    return acc


def _ag(v, ax):
    n = SIZES[ax]
    i = lax.axis_index(ax)
    parts = [v] + [_shift(v, ax, k) for k in range(1, n)]
    rel = jnp.stack(parts)
    idx = (i - jnp.arange(n)) % n
    return rel[idx]


def _rs_dp(part, dt):
    R, N = part.shape
    a = part.reshape(SIZES["y"], SIZES["x"], SIZES["core"], R // 32, N)
    a = _rs(a, "core", 2, dt)
    a = _rs(a, "x", 1, dt)
    a = _rs(a, "y", 0, dt)
    return a


def _score_kernel(u_ref, n_ref, s_ref, k_ref, col_ref, rs_ref):
    j = pl.program_id(0)
    sc = jnp.dot(u_ref[...], n_ref[...], preferred_element_type=F32)
    s = jnp.exp(sc * (1.0 / soft_temp))
    s_ref[...] = s
    k = s * s
    k_ref[:, pl.ds(pl.multiple_of(j * s.shape[1], s.shape[1]), s.shape[1])] = k.astype(BF16)
    col_ref[...] = jnp.sum(k, axis=0, keepdims=True)

    @pl.when(j == 0)
    def _():
        rs_ref[...] = jnp.zeros_like(rs_ref)

    rs_ref[...] += jnp.sum(s, axis=1, keepdims=True)


def _scores(unit_b, normed, bp=1024):
    T, E = unit_b.shape
    Pn = normed.shape[1]
    soft, kb, col, rs = pl.pallas_call(
        _score_kernel,
        grid=(Pn // bp,),
        in_specs=[pl.BlockSpec((T, E), lambda j: (0, 0)), pl.BlockSpec((E, bp), lambda j: (0, j))],
        out_specs=[
            pl.BlockSpec((T, bp), lambda j: (0, j)),
            pl.BlockSpec(memory_space=pltpu.VMEM),
            pl.BlockSpec((1, bp), lambda j: (0, j)),
            pl.BlockSpec((T, 1), lambda j: (0, 0)),
        ],
        out_shape=[
            jax.ShapeDtypeStruct((T, Pn), F32),
            jax.ShapeDtypeStruct((T, Pn), BF16),
            jax.ShapeDtypeStruct((1, Pn), F32),
            jax.ShapeDtypeStruct((T, 1), F32),
        ],
    )(unit_b, normed)
    return soft, kb, col[0], rs[:, 0]


def _split(v):
    hi = v.astype(BF16)
    lo = (v - hi.astype(F32)).astype(BF16)
    return jnp.stack([hi, lo])


def _colpass(kern_b, r):
    out = jnp.dot(_split(r), kern_b, preferred_element_type=F32)
    return out[0] + out[1]


def _rowpass(kern_b, c):
    out = jnp.dot(kern_b, _split(c).T, preferred_element_type=F32)
    return out[:, 0] + out[:, 1]


def on_device(features, head_weight, prototypes):
    partial_proj = jnp.dot(features, head_weight, preferred_element_type=F32)
    T, E = partial_proj.shape
    nz = SIZES["z"]
    proj_blk = _rs(partial_proj.reshape(nz, T // nz, E), "z", 0)
    projected = _ag(proj_blk, "z").reshape(T, E)
    length = jnp.sqrt(jnp.sum(projected * projected, axis=1, keepdims=True) + 1e-06)
    unit = projected / length
    unit_b = unit.astype(BF16)
    proto_f = prototypes.astype(F32)
    normed = (proto_f / jnp.sqrt(jnp.sum(proto_f * proto_f, axis=0, keepdims=True) + 1e-06)).astype(BF16)
    soft, kern_b, col0, soft_local = _scores(unit_b, normed)
    kern = soft * soft
    r = None
    soft_total = None
    for step in range(ITERS):
        colpart = col0 if r is None else _colpass(kern_b, r)
        c = 1.0 / _allsum_dp(colpart)
        rowpart = _rowpass(kern_b, c)
        if step == 0:
            both = _allsum(jnp.stack([rowpart, soft_local]), "z")
            row, soft_total = both[0], both[1]
        else:
            row = _allsum(rowpart, "z")
        r = 1.0 / row
    plan = kern * c[None, :] * r[:, None]
    probs = soft / soft_total[:, None]
    codes = (PROTOS * plan).astype(BF16)
    tokens_all = 32 * T
    factor = PROTOS / (soft_temp * math.sqrt(tokens_all))
    dscore = ((probs - plan) * factor).astype(BF16)
    half = dscore.shape[1] // 2
    pg = []
    for h in range(2):
        pg_part = lax.dot_general(
            unit_b, dscore[:, h * half:(h + 1) * half], (((0,), (0,)), ((), ())), preferred_element_type=F32
        )
        pg.append(_rs_dp(pg_part, BF16))
    proto_grad = jnp.concatenate(pg, axis=1)
    dunit_part = lax.dot_general(dscore, normed, (((1,), (1,)), ((), ())), preferred_element_type=F32)
    dunit = _allsum(dunit_part, "z", BF16)
    dproj = ((dunit - unit * jnp.sum(unit * dunit, axis=1, keepdims=True)) / length).astype(BF16)
    head_part = lax.dot_general(dproj, features, (((0,), (0,)), ((), ())), preferred_element_type=F32)
    head_grad = _rs_dp(head_part, BF16)
    return (codes, proto_grad, head_grad)


def solution(mesh):
    devs = mesh.devices.reshape(SIZES["y"], SIZES["x"], SIZES["core"], SIZES["z"])
    m4 = Mesh(devs, ("y", "x", "core", "z"))
    in_specs = (P(DP, "z"), P("z", None), P(None, "z"))
    out_specs = (P(DP, "z"), P(DP, "z"), P(DP, "z"))

    return jax.shard_map(on_device, mesh=m4, in_specs=in_specs, out_specs=out_specs, check_vma=False)
```

```python
import math

import jax
import jax.numpy as jnp
from jax import lax
from jax.experimental import pallas as pl
from jax.experimental.pallas import tpu as pltpu
from jax.sharding import Mesh
from jax.sharding import PartitionSpec as P

PROTOS = 32768
ITERS = 3


soft_temp = 0.1

DP = ("y", "x", "core")
SIZES = {"y": 4, "x": 4, "core": 2, "z": 4}
F32 = jnp.float32
BF16 = jnp.bfloat16


def _shift(v, ax, k):
    n = SIZES[ax]
    return lax.ppermute(v, ax, [(i, (i + k) % n) for i in range(n)])


def _allsum(v, ax, dt=None):
    sent = v if dt is None else v.astype(dt)
    acc = v
    for k in range(1, SIZES[ax]):
        acc = acc + _shift(sent, ax, k).astype(v.dtype)
    return acc


def _allsum_dp(v):
    for ax in ("core", "x", "y"):
        v = _allsum(v, ax)
    return v


def _rs(a, ax, axis, dt=None):
    n = SIZES[ax]
    i = lax.axis_index(ax)
    acc = lax.dynamic_index_in_dim(a, i, axis, keepdims=False)
    for k in range(1, n):
        blk = lax.dynamic_index_in_dim(a, (i + k) % n, axis, keepdims=False)
        if dt is not None:
            blk = blk.astype(dt)
        acc = acc + _shift(blk, ax, k).astype(a.dtype)
    return acc


def _ag(v, ax):
    n = SIZES[ax]
    i = lax.axis_index(ax)
    parts = [v] + [_shift(v, ax, k) for k in range(1, n)]
    rel = jnp.stack(parts)
    idx = (i - jnp.arange(n)) % n
    return rel[idx]


def _rs_dp(part, dt):
    R, N = part.shape
    a = part.reshape(SIZES["y"], SIZES["x"], SIZES["core"], R // 32, N)
    a = _rs(a, "core", 2, dt)
    a = _rs(a, "x", 1, dt)
    a = _rs(a, "y", 0, dt)
    return a


def _score_kernel(u_ref, n_ref, s_ref, k_ref, col_ref, rs_ref):
    j = pl.program_id(0)
    sc = jnp.dot(u_ref[...], n_ref[...], preferred_element_type=F32)
    s = jnp.exp(sc * (1.0 / soft_temp))
    s_ref[...] = s
    k = s * s
    k_ref[:, pl.ds(pl.multiple_of(j * s.shape[1], s.shape[1]), s.shape[1])] = k.astype(BF16)
    col_ref[...] = jnp.sum(k, axis=0, keepdims=True)

    @pl.when(j == 0)
    def _():
        rs_ref[...] = jnp.zeros_like(rs_ref)

    rs_ref[...] += jnp.sum(s, axis=1, keepdims=True)


def _scores(unit_b, normed, bp=1024):
    T, E = unit_b.shape
    Pn = normed.shape[1]
    soft, kb, col, rs = pl.pallas_call(
        _score_kernel,
        grid=(Pn // bp,),
        in_specs=[pl.BlockSpec((T, E), lambda j: (0, 0)), pl.BlockSpec((E, bp), lambda j: (0, j))],
        out_specs=[
            pl.BlockSpec((T, bp), lambda j: (0, j)),
            pl.BlockSpec(memory_space=pltpu.VMEM),
            pl.BlockSpec((1, bp), lambda j: (0, j)),
            pl.BlockSpec((T, 1), lambda j: (0, 0)),
        ],
        out_shape=[
            jax.ShapeDtypeStruct((T, Pn), F32),
            jax.ShapeDtypeStruct((T, Pn), BF16),
            jax.ShapeDtypeStruct((1, Pn), F32),
            jax.ShapeDtypeStruct((T, 1), F32),
        ],
    )(unit_b, normed)
    return soft, kb, col[0], rs[:, 0]


def _split(v):
    hi = v.astype(BF16)
    lo = (v - hi.astype(F32)).astype(BF16)
    return jnp.stack([hi, lo])


def _colpass(kern_b, r):
    out = jnp.dot(_split(r), kern_b, preferred_element_type=F32)
    return out[0] + out[1]


def _rowpass(kern_b, c):
    out = jnp.dot(kern_b, _split(c).T, preferred_element_type=F32)
    return out[:, 0] + out[:, 1]


def on_device(features, head_weight, prototypes):
    partial_proj = jnp.dot(features, head_weight, preferred_element_type=F32)
    T, E = partial_proj.shape
    nz = SIZES["z"]
    proj_blk = _rs(partial_proj.reshape(nz, T // nz, E), "z", 0)
    projected = _ag(proj_blk, "z").reshape(T, E)
    length = jnp.sqrt(jnp.sum(projected * projected, axis=1, keepdims=True) + 1e-06)
    unit = projected / length
    unit_b = unit.astype(BF16)
    proto_f = prototypes.astype(F32)
    normed = (proto_f / jnp.sqrt(jnp.sum(proto_f * proto_f, axis=0, keepdims=True) + 1e-06)).astype(BF16)
    soft, kern_b, col0, soft_local = _scores(unit_b, normed)
    kern = soft * soft
    c = 1.0 / _allsum_dp(col0)
    rowpart = _rowpass(kern_b, c)
    both = _allsum(jnp.stack([rowpart, soft_local]), "z")
    r, soft_total = 1.0 / both[0], both[1]

    def sinkhorn_step(_, cr):
        c, r = cr
        c = 1.0 / _allsum_dp(_colpass(kern_b, r))
        r = 1.0 / _allsum(_rowpass(kern_b, c), "z")
        return c, r

    c, r = lax.fori_loop(1, ITERS, sinkhorn_step, (c, r))
    plan = kern * c[None, :] * r[:, None]
    probs = soft / soft_total[:, None]
    codes = (PROTOS * plan).astype(BF16)
    tokens_all = 32 * T
    factor = PROTOS / (soft_temp * math.sqrt(tokens_all))
    dscore = ((probs - plan) * factor).astype(BF16)
    half = dscore.shape[1] // 2
    pg = []
    for h in range(2):
        pg_part = lax.dot_general(
            unit_b, dscore[:, h * half:(h + 1) * half], (((0,), (0,)), ((), ())), preferred_element_type=F32
        )
        pg.append(_rs_dp(pg_part, BF16))
    proto_grad = jnp.concatenate(pg, axis=1)
    dunit_part = lax.dot_general(dscore, normed, (((1,), (1,)), ((), ())), preferred_element_type=F32)
    dunit = _allsum(dunit_part, "z", BF16)
    dproj = ((dunit - unit * jnp.sum(unit * dunit, axis=1, keepdims=True)) / length).astype(BF16)
    head_part = lax.dot_general(dproj, features, (((0,), (0,)), ((), ())), preferred_element_type=F32)
    head_grad = _rs_dp(head_part, BF16)
    return (codes, proto_grad, head_grad)


def solution(mesh):
    devs = mesh.devices.reshape(SIZES["y"], SIZES["x"], SIZES["core"], SIZES["z"])
    m4 = Mesh(devs, ("y", "x", "core", "z"))
    in_specs = (P(DP, "z"), P("z", None), P(None, "z"))
    out_specs = (P(DP, "z"), P(DP, "z"), P(DP, "z"))

    return jax.shard_map(on_device, mesh=m4, in_specs=in_specs, out_specs=out_specs, check_vma=False)
```

```python
import math

import jax
import jax.numpy as jnp
from jax import lax
from jax.experimental import pallas as pl
from jax.experimental.pallas import tpu as pltpu
from jax.sharding import Mesh
from jax.sharding import PartitionSpec as P

PROTOS = 32768
ITERS = 3


soft_temp = 0.1

DP = ("y", "x", "core")
SIZES = {"y": 4, "x": 4, "core": 2, "z": 4}
F32 = jnp.float32
BF16 = jnp.bfloat16


def _shift(v, ax, k):
    n = SIZES[ax]
    return lax.ppermute(v, ax, [(i, (i + k) % n) for i in range(n)])


def _allsum(v, ax, dt=None):
    sent = v if dt is None else v.astype(dt)
    acc = v
    for k in range(1, SIZES[ax]):
        acc = acc + _shift(sent, ax, k).astype(v.dtype)
    return acc


def _allsum_dp(v):
    for ax in ("core", "x", "y"):
        v = _allsum(v, ax)
    return v


def _rs(a, ax, axis, dt=None):
    n = SIZES[ax]
    i = lax.axis_index(ax)
    acc = lax.dynamic_index_in_dim(a, i, axis, keepdims=False)
    for k in range(1, n):
        blk = lax.dynamic_index_in_dim(a, (i + k) % n, axis, keepdims=False)
        if dt is not None:
            blk = blk.astype(dt)
        acc = acc + _shift(blk, ax, k).astype(a.dtype)
    return acc


def _ag(v, ax):
    n = SIZES[ax]
    i = lax.axis_index(ax)
    parts = [v] + [_shift(v, ax, k) for k in range(1, n)]
    rel = jnp.stack(parts)
    idx = (i - jnp.arange(n)) % n
    return rel[idx]


def _rs_dp(part, dt):
    R, N = part.shape
    a = part.reshape(SIZES["y"], SIZES["x"], SIZES["core"], R // 32, N)
    a = _rs(a, "core", 2, dt)
    a = _rs(a, "x", 1, dt)
    a = _rs(a, "y", 0, dt)
    return a


def _score_kernel(u_ref, n_ref, s_ref, k_ref, col_ref, rs_ref):
    j = pl.program_id(0)
    sc = jnp.dot(u_ref[...], n_ref[...], preferred_element_type=F32)
    s = jnp.exp(sc * (1.0 / soft_temp))
    s_ref[...] = s
    k = s * s
    k_ref[:, pl.ds(pl.multiple_of(j * s.shape[1], s.shape[1]), s.shape[1])] = k.astype(BF16)
    col_ref[...] = jnp.sum(k, axis=0, keepdims=True)

    @pl.when(j == 0)
    def _():
        rs_ref[...] = jnp.zeros_like(rs_ref)

    rs_ref[...] += jnp.sum(s, axis=1, keepdims=True)


def _scores(unit_b, normed, bp=1024):
    T, E = unit_b.shape
    Pn = normed.shape[1]
    soft, kb, col, rs = pl.pallas_call(
        _score_kernel,
        grid=(Pn // bp,),
        in_specs=[pl.BlockSpec((T, E), lambda j: (0, 0)), pl.BlockSpec((E, bp), lambda j: (0, j))],
        out_specs=[
            pl.BlockSpec((T, bp), lambda j: (0, j)),
            pl.BlockSpec(memory_space=pltpu.VMEM),
            pl.BlockSpec((1, bp), lambda j: (0, j)),
            pl.BlockSpec((T, 1), lambda j: (0, 0)),
        ],
        out_shape=[
            jax.ShapeDtypeStruct((T, Pn), F32),
            jax.ShapeDtypeStruct((T, Pn), BF16),
            jax.ShapeDtypeStruct((1, Pn), F32),
            jax.ShapeDtypeStruct((T, 1), F32),
        ],
    )(unit_b, normed)
    return soft, kb, col[0], rs[:, 0]


def _split(v):
    hi = v.astype(BF16)
    lo = (v - hi.astype(F32)).astype(BF16)
    return jnp.stack([hi, lo])


def _colpass(kern_b, r):
    out = jnp.dot(_split(r), kern_b, preferred_element_type=F32)
    return out[0] + out[1]


def _rowpass(kern_b, c):
    out = jnp.dot(kern_b, _split(c).T, preferred_element_type=F32)
    return out[:, 0] + out[:, 1]


def on_device(features, head_weight, prototypes):
    partial_proj = jnp.dot(features, head_weight, preferred_element_type=F32)
    T, E = partial_proj.shape
    nz = SIZES["z"]
    proj_blk = _rs(partial_proj.reshape(nz, T // nz, E), "z", 0)
    projected = _ag(proj_blk, "z").reshape(T, E)
    length = jnp.sqrt(jnp.sum(projected * projected, axis=1, keepdims=True) + 1e-06)
    unit = projected / length
    unit_b = unit.astype(BF16)
    proto_f = prototypes.astype(F32)
    normed = (proto_f / jnp.sqrt(jnp.sum(proto_f * proto_f, axis=0, keepdims=True) + 1e-06)).astype(BF16)
    soft, kern_b, col0, soft_local = _scores(unit_b, normed)
    kern = soft * soft
    c = 1.0 / _allsum_dp(col0)
    rowpart = _rowpass(kern_b, c)
    both = _allsum(jnp.stack([rowpart, soft_local]), "z")
    r, soft_total = 1.0 / both[0], both[1]

    def sinkhorn_step(_, cr):
        c, r = cr
        c = 1.0 / _allsum_dp(_colpass(kern_b, r))
        r = 1.0 / _allsum(_rowpass(kern_b, c), "z")
        return c, r

    c, r = lax.fori_loop(1, ITERS, sinkhorn_step, (c, r))
    plan = kern * c[None, :] * r[:, None]
    probs = soft / soft_total[:, None]
    codes = (PROTOS * plan).astype(BF16)
    tokens_all = 32 * T
    factor = PROTOS / (soft_temp * math.sqrt(tokens_all))
    dscore = ((probs - plan) * factor).astype(BF16)
    half = dscore.shape[1] // 2
    pg0 = lax.dot_general(unit_b, dscore[:, :half], (((0,), (0,)), ((), ())), preferred_element_type=F32)
    rs0 = _rs_dp(pg0, BF16)
    pg1 = lax.dot_general(unit_b, dscore[:, half:], (((0,), (0,)), ((), ())), preferred_element_type=F32)
    dunit_part = lax.dot_general(dscore, normed, (((1,), (1,)), ((), ())), preferred_element_type=F32)
    dunit = _allsum(dunit_part, "z", BF16)
    dproj = ((dunit - unit * jnp.sum(unit * dunit, axis=1, keepdims=True)) / length).astype(BF16)
    head_part = lax.dot_general(dproj, features, (((0,), (0,)), ((), ())), preferred_element_type=F32)
    rs1 = _rs_dp(jnp.concatenate([pg1, head_part], axis=1), BF16)
    proto_grad = jnp.concatenate([rs0, rs1[:, :half]], axis=1)
    return (codes, proto_grad, rs1[:, half:])


def solution(mesh):
    devs = mesh.devices.reshape(SIZES["y"], SIZES["x"], SIZES["core"], SIZES["z"])
    m4 = Mesh(devs, ("y", "x", "core", "z"))
    in_specs = (P(DP, "z"), P("z", None), P(None, "z"))
    out_specs = (P(DP, "z"), P(DP, "z"), P(DP, "z"))

    return jax.shard_map(on_device, mesh=m4, in_specs=in_specs, out_specs=out_specs, check_vma=False)
```

```python
import math

import jax
import jax.numpy as jnp
from jax import lax
from jax.experimental import pallas as pl
from jax.experimental.pallas import tpu as pltpu
from jax.sharding import Mesh
from jax.sharding import PartitionSpec as P

PROTOS = 32768
ITERS = 3


soft_temp = 0.1

DP = ("y", "x", "core")
SIZES = {"y": 4, "x": 4, "core": 2, "z": 4}
F32 = jnp.float32
BF16 = jnp.bfloat16


def _shift(v, ax, k):
    n = SIZES[ax]
    return lax.ppermute(v, ax, [(i, (i + k) % n) for i in range(n)])


def _allsum(v, ax, dt=None):
    sent = v if dt is None else v.astype(dt)
    acc = v
    for k in range(1, SIZES[ax]):
        acc = acc + _shift(sent, ax, k).astype(v.dtype)
    return acc


def _allsum_dp(v):
    for ax in ("core", "x", "y"):
        v = _allsum(v, ax)
    return v


def _rs(a, ax, axis, dt=None):
    n = SIZES[ax]
    i = lax.axis_index(ax)
    acc = lax.dynamic_index_in_dim(a, i, axis, keepdims=False)
    for k in range(1, n):
        blk = lax.dynamic_index_in_dim(a, (i + k) % n, axis, keepdims=False)
        if dt is not None:
            blk = blk.astype(dt)
        acc = acc + _shift(blk, ax, k).astype(a.dtype)
    return acc


def _ag(v, ax):
    n = SIZES[ax]
    i = lax.axis_index(ax)
    parts = [v] + [_shift(v, ax, k) for k in range(1, n)]
    rel = jnp.stack(parts)
    idx = (i - jnp.arange(n)) % n
    return rel[idx]


def _rs_dp(part, dt):
    R, N = part.shape
    a = part.reshape(SIZES["y"], SIZES["x"], SIZES["core"], R // 32, N)
    a = _rs(a, "core", 2, dt)
    a = _rs(a, "x", 1, dt)
    a = _rs(a, "y", 0, dt)
    return a


def _score_kernel(u_ref, n_ref, s_ref, k_ref, col_ref, rs_ref):
    j = pl.program_id(0)
    sc = jnp.dot(u_ref[...], n_ref[...], preferred_element_type=F32)
    s = jnp.exp(sc * (1.0 / soft_temp))
    s_ref[...] = s
    k = s * s
    k_ref[:, pl.ds(pl.multiple_of(j * s.shape[1], s.shape[1]), s.shape[1])] = k.astype(BF16)
    col_ref[...] = jnp.sum(k, axis=0, keepdims=True)

    @pl.when(j == 0)
    def _():
        rs_ref[...] = jnp.zeros_like(rs_ref)

    rs_ref[...] += jnp.sum(s, axis=1, keepdims=True)


def _scores(unit_b, normed, bp=1024):
    T, E = unit_b.shape
    Pn = normed.shape[1]
    soft, kb, col, rs = pl.pallas_call(
        _score_kernel,
        grid=(Pn // bp,),
        in_specs=[pl.BlockSpec((T, E), lambda j: (0, 0)), pl.BlockSpec((E, bp), lambda j: (0, j))],
        out_specs=[
            pl.BlockSpec((T, bp), lambda j: (0, j)),
            pl.BlockSpec(memory_space=pltpu.VMEM),
            pl.BlockSpec((1, bp), lambda j: (0, j)),
            pl.BlockSpec((T, 1), lambda j: (0, 0)),
        ],
        out_shape=[
            jax.ShapeDtypeStruct((T, Pn), F32),
            jax.ShapeDtypeStruct((T, Pn), BF16),
            jax.ShapeDtypeStruct((1, Pn), F32),
            jax.ShapeDtypeStruct((T, 1), F32),
        ],
    )(unit_b, normed)
    return soft, kb, col[0], rs[:, 0]


def _split(v):
    hi = v.astype(BF16)
    lo = (v - hi.astype(F32)).astype(BF16)
    return jnp.stack([hi, lo])


def _colpass(kern_b, r):
    out = jnp.dot(_split(r), kern_b, preferred_element_type=F32)
    return out[0] + out[1]


def _rowpass(kern_b, c):
    out = jnp.dot(kern_b, _split(c).T, preferred_element_type=F32)
    return out[:, 0] + out[:, 1]


def on_device(features, head_weight, prototypes):
    partial_proj = jnp.dot(features, head_weight, preferred_element_type=F32)
    T, E = partial_proj.shape
    nz = SIZES["z"]
    proj_blk = _rs(partial_proj.reshape(nz, T // nz, E), "z", 0)
    projected = _ag(proj_blk, "z").reshape(T, E)
    length = jnp.sqrt(jnp.sum(projected * projected, axis=1, keepdims=True) + 1e-06)
    unit = projected / length
    unit_b = unit.astype(BF16)
    proto_f = prototypes.astype(F32)
    normed = (proto_f / jnp.sqrt(jnp.sum(proto_f * proto_f, axis=0, keepdims=True) + 1e-06)).astype(BF16)
    soft, kern_b, col0, soft_local = _scores(unit_b, normed)
    kern = soft * soft
    c = 1.0 / _allsum_dp(col0)
    rowpart = _rowpass(kern_b, c)
    both = _allsum(jnp.stack([rowpart, soft_local]), "z")
    r, soft_total = 1.0 / both[0], both[1]

    def sinkhorn_step(_, cr):
        c, r = cr
        c = 1.0 / _allsum_dp(_colpass(kern_b, r))
        r = 1.0 / _allsum(_rowpass(kern_b, c), "z")
        return c, r

    c, r = lax.fori_loop(1, ITERS, sinkhorn_step, (c, r))
    plan = kern * c[None, :] * r[:, None]
    probs = soft / soft_total[:, None]
    codes = (PROTOS * plan).astype(BF16)
    tokens_all = 32 * T
    factor = PROTOS / (soft_temp * math.sqrt(tokens_all))
    dscore = ((probs - plan) * factor).astype(BF16)
    half = dscore.shape[1] * 3 // 4
    pg0 = lax.dot_general(unit_b, dscore[:, :half], (((0,), (0,)), ((), ())), preferred_element_type=F32)
    rs0 = _rs_dp(pg0, BF16)
    pg1 = lax.dot_general(unit_b, dscore[:, half:], (((0,), (0,)), ((), ())), preferred_element_type=F32)
    dunit_part = lax.dot_general(dscore, normed, (((1,), (1,)), ((), ())), preferred_element_type=F32)
    dunit = _allsum(dunit_part, "z", BF16)
    dproj = ((dunit - unit * jnp.sum(unit * dunit, axis=1, keepdims=True)) / length).astype(BF16)
    head_part = lax.dot_general(dproj, features, (((0,), (0,)), ((), ())), preferred_element_type=F32)
    rs1 = _rs_dp(jnp.concatenate([pg1, head_part], axis=1), BF16)
    w1 = dscore.shape[1] - half
    proto_grad = jnp.concatenate([rs0, rs1[:, :w1]], axis=1)
    return (codes, proto_grad, rs1[:, w1:])


def solution(mesh):
    devs = mesh.devices.reshape(SIZES["y"], SIZES["x"], SIZES["core"], SIZES["z"])
    m4 = Mesh(devs, ("y", "x", "core", "z"))
    in_specs = (P(DP, "z"), P("z", None), P(None, "z"))
    out_specs = (P(DP, "z"), P(DP, "z"), P(DP, "z"))

    return jax.shard_map(on_device, mesh=m4, in_specs=in_specs, out_specs=out_specs, check_vma=False)
```
